256 devices in a mesh: ent: 64 (over z, y, core), rep: 4 (over x).
Axes of the slice: x: 4, y: 4, z: 8, core: 2. Of those that a mesh axis runs over, the one named last changes fastest.
Arguments:
- table: float32 [262144, 256], P('ent'), may hold values from -6.1 to 6.1
- relations: float32 [824, 256], P('rep'), may hold values from -4 to 4
- anchor: int32 [2048], P('rep'), may hold values from 0 to 262143
- rel_one: int32 [2048], P('rep'), may hold values from 0 to 823
- rel_two: int32 [2048], P('rep'), may hold values from 0 to 823
Outputs:
- log_answer: float32 [2048, 262144], P('rep', 'ent')
The draws below stay inside these ranges and needn't reach their ends.
All inputs are finite; a program needn't handle non-finite values.
Results may differ from the reference program's by a relative error of at most 0.00018.
Values sent between devices are 32-bit elements; how exact they have to be, the bound alone decides.
No kernel may reach another device: no remote copies, remote signals or barrier semaphores. Data moves between devices by JAX's collectives and lax.ppermute only.
A program may use at most 128 MiB of HBM per device.

```python
import math
import jax
import jax.numpy as jnp
from jax import lax

RANK = 128
NREL = 824
ENTITIES = 262144
QUERIES = 2048


def draw_table(key, part):
    first = jax.random.fold_in(jax.random.fold_in(key, 11), 0)
    base = jnp.clip(jax.random.normal(first, (ENTITIES, 2 * RANK), jnp.float32), -6.0, 6.0)
    return (0.35 * base).astype(jnp.float32)


def touch_ends(values, stream_key, low, largest):
    longest = values.shape.index(max(values.shape))
    spots = []
    for shift in (0, 1):
        where = [jax.random.randint(jax.random.fold_in(stream_key, axis), (), 0, length) for axis, length in enumerate(values.shape)]
        where[longest] = (where[longest] + shift) % values.shape[longest]
        spots.append(tuple(where))
    return values.at[spots[0]].set(low).at[spots[1]].set(largest)


def block_scale(own_key, extent, pieces, low, largest):
    level, own = 1.0, jax.random.fold_in(own_key, 6)
    for axis_at, parts in pieces:
        steps = jnp.exp(jax.random.uniform(jax.random.fold_in(own, axis_at), (parts,), jnp.float32, low / len(pieces), largest / len(pieces)))
        level = level * jnp.repeat(steps, extent[axis_at] // parts).reshape([-1 if axis == axis_at else 1 for axis in range(len(extent))])
    return level


def normal_values(stream_key, dims, deviation, reach, cuts=(), held_as=jnp.bfloat16):
    gain = block_scale(stream_key, dims, cuts, -0.22, 0.18) if cuts else 1.0
    array = jax.random.normal(stream_key, dims, jnp.float32) * deviation * gain
    return jnp.minimum(jnp.maximum(array, -reach), reach).astype(held_as)


def setup_inputs(seed: int = 0) -> dict:
    key_of = jax.random.split(jax.random.key(seed), 6)
    return {
        "table": draw_table(jax.random.fold_in(key_of[5], 71), 0),
        "relations": normal_values(key_of[1], (NREL, 2 * RANK), 1.0, 4.0, ((0, 4),), jnp.float32),
        "anchor": touch_ends(jax.random.randint(key_of[2], (QUERIES,), 0, ENTITIES), jax.random.fold_in(key_of[2], 1), 0, ENTITIES - 1).astype(jnp.int32),
        "rel_one": touch_ends(jax.random.randint(key_of[3], (QUERIES,), 0, NREL), jax.random.fold_in(key_of[3], 1), 0, NREL - 1).astype(jnp.int32),
        "rel_two": touch_ends(jax.random.randint(key_of[4], (QUERIES,), 0, NREL), jax.random.fold_in(key_of[4], 1), 0, NREL - 1).astype(jnp.int32),
    }


def cmul(left, right):
    half = left.shape[1] // 2
    lre, lim = left[:, :half], left[:, half:]
    rre, rim = right[:, :half], right[:, half:]
    return jnp.concatenate([lre * rre - lim * rim, lre * rim + lim * rre], axis=1)


def reference(table, relations, anchor, rel_one, rel_two):
    highest = lax.Precision.HIGHEST
    query_one = cmul(table[anchor], relations[rel_one])
    rel_second = relations[rel_two]
    block = math.gcd(QUERIES, 128)
    count = QUERIES // block

    def one_block(pair):
        query, second = pair
        scores = jnp.dot(query, table.T, precision=highest, preferred_element_type=jnp.float32)
        peak = jnp.max(scores, axis=1, keepdims=True)
        weights = jnp.exp(scores - peak)
        prob = weights / jnp.sum(weights, axis=1, keepdims=True)
        expected = jnp.dot(prob, table, precision=highest, preferred_element_type=jnp.float32)
        query_two = cmul(expected, second)
        scores_two = jnp.dot(query_two, table.T, precision=highest, preferred_element_type=jnp.float32)
        peak_two = jnp.max(scores_two, axis=1, keepdims=True)
        shifted = scores_two - peak_two
        return shifted - jnp.log(jnp.sum(jnp.exp(shifted), axis=1, keepdims=True))

    result = lax.map(one_block, (query_one.reshape(count, block, -1), rel_second.reshape(count, block, -1)))
    return result.reshape(QUERIES, ENTITIES)
```

```python
import jax
import jax.numpy as jnp
from jax import lax
from jax.sharding import PartitionSpec as P


def cmul(left, right):
    half = left.shape[1] // 2
    lre, lim = (left[:, :half], left[:, half:])
    rre, rim = (right[:, :half], right[:, half:])
    return jnp.concatenate([lre * rre - lim * rim, lre * rim + lim * rre], axis=1)


def against(query, table):
    return lax.dot_general(
        query,
        table,
        (((1,), (1,)), ((), ())),
        precision=lax.Precision.HIGHEST,
        preferred_element_type=jnp.float32,
    )


def weighted(weights, table):
    return jnp.dot(
        weights, table, precision=lax.Precision.HIGHEST, preferred_element_type=jnp.float32
    )


def partner(size, bit):
    return [(i, i ^ (1 << bit)) for i in range(size)]


def scatter_rounds(state, combine, size, idx):
    offset = 0
    for bit in range(size.bit_length() - 1):
        rows = state[0].shape[0] // 2
        side = (idx >> bit) & 1
        keep = tuple(lax.dynamic_slice_in_dim(x, side * rows, rows, 0) for x in state)
        send = tuple(lax.dynamic_slice_in_dim(x, (1 - side) * rows, rows, 0) for x in state)
        recv = lax.ppermute(send, "ent", partner(size, bit))
        state = combine(keep, recv)
        offset = offset + side * rows
    return state, offset


def gather_rounds(block, size, idx):
    for bit in reversed(range(size.bit_length() - 1)):
        side = (idx >> bit) & 1
        recv = lax.ppermute(block, "ent", partner(size, bit))
        low = jnp.where(side == 0, block, recv)
        high = jnp.where(side == 0, recv, block)
        block = jnp.concatenate([low, high], axis=0)
    return block


def add_pair(a, b):
    return tuple(x + y for x, y in zip(a, b))


def softmax_pair(a, b):
    wa, sa, ma = a
    wb, sb, mb = b
    top = jnp.maximum(ma, mb)
    fa = jnp.exp(ma - top)
    fb = jnp.exp(mb - top)
    return (wa * fa + wb * fb, sa * fa + sb * fb, top)


def make_body(size):
    def on_device(table, relations, anchor, rel_one, rel_two):
        rows = table.shape[0]
        idx = lax.axis_index("ent")
        start = idx * rows
        offset = anchor - start
        inside = ((offset >= 0) & (offset < rows)).astype(jnp.float32)
        local_rows = jnp.take(table, jnp.clip(offset, 0, rows - 1), axis=0) * inside[:, None]
        rel_all = lax.all_gather(relations, "rep", axis=0, tiled=True)
        rel_first = jnp.take(rel_all, rel_one, axis=0)
        rel_second = jnp.take(rel_all, rel_two, axis=0)

        (anchor_block,), at = scatter_rounds((local_rows,), add_pair, size, idx)
        block = anchor_block.shape[0]
        query_block = cmul(anchor_block, lax.dynamic_slice_in_dim(rel_first, at, block, 0))
        query_one = gather_rounds(query_block, size, idx)

        scores = against(query_one, table)
        peak = jnp.max(scores, axis=1, keepdims=True)
        weights = jnp.exp(scores - peak)
        total = jnp.sum(weights, axis=1, keepdims=True)
        summed = weighted(weights, table)
        (summed, total, _), at = scatter_rounds((summed, total, peak), softmax_pair, size, idx)
        expected = summed / total
        query_two = gather_rounds(
            cmul(expected, lax.dynamic_slice_in_dim(rel_second, at, block, 0)), size, idx
        )

        scores_two = against(query_two, table)
        top = jnp.max(scores_two, axis=1, keepdims=True)
        mass = jnp.sum(jnp.exp(scores_two - top), axis=1, keepdims=True)
        for bit in range(size.bit_length() - 1):
            other_mass, other_top = lax.ppermute((mass, top), "ent", partner(size, bit))
            both = jnp.maximum(top, other_top)
            mass = mass * jnp.exp(top - both) + other_mass * jnp.exp(other_top - both)
            top = both
        return (scores_two - top) - jnp.log(mass)

    return on_device


def solution(mesh):
    size = mesh.shape["ent"]
    assert size & (size - 1) == 0
    in_specs = (P("ent", None), P("rep", None), P("rep"), P("rep"), P("rep"))
    out_specs = P("rep", "ent")
    return jax.shard_map(
        make_body(size), mesh=mesh, in_specs=in_specs, out_specs=out_specs, check_vma=False
    )
```

```python
import jax
import jax.numpy as jnp
from jax import lax
from jax.sharding import PartitionSpec as P


def cmul(left, right):
    half = left.shape[1] // 2
    lre, lim = (left[:, :half], left[:, half:])
    rre, rim = (right[:, :half], right[:, half:])
    return jnp.concatenate([lre * rre - lim * rim, lre * rim + lim * rre], axis=1)


def against(query, table):
    return lax.dot_general(
        query,
        table,
        (((1,), (1,)), ((), ())),
        precision=lax.Precision.HIGHEST,
        preferred_element_type=jnp.float32,
    )


def weighted(weights, table):
    return jnp.dot(
        weights, table, precision=lax.Precision.HIGHEST, preferred_element_type=jnp.float32
    )


def partner(size, bit):
    return [(i, i ^ (1 << bit)) for i in range(size)]


def scatter_rounds(state, combine, bits, idx, axis):
    offset = 0
    for bit in bits:
        rows = state.shape[0] // 2
        side = (idx >> bit) & 1
        keep = lax.dynamic_slice_in_dim(state, side * rows, rows, 0)
        send = lax.dynamic_slice_in_dim(state, (1 - side) * rows, rows, 0)
        state = combine(keep, lax.ppermute(send, axis, partner(axis_size(axis), bit)))
        offset = offset + side * rows
    return state, offset


def doubling_rounds(state, combine, bits, axis):
    for bit in bits:
        state = combine(state, lax.ppermute(state, axis, partner(axis_size(axis), bit)))
    return state


def gather_rounds(block, bits, idx, axis):
    for bit in reversed(bits):
        side = (idx >> bit) & 1
        recv = lax.ppermute(block, axis, partner(axis_size(axis), bit))
        low = jnp.where(side == 0, block, recv)
        high = jnp.where(side == 0, recv, block)
        block = jnp.concatenate([low, high], axis=0)
    return block


SIZES = {}


def axis_size(axis):
    return SIZES[axis]


def add_pair(a, b):
    return a + b


def softmax_pair(a, b):
    top = jnp.maximum(a[:, -1:], b[:, -1:])
    fa = jnp.exp(a[:, -1:] - top)
    fb = jnp.exp(b[:, -1:] - top)
    return jnp.concatenate([a[:, :-1] * fa + b[:, :-1] * fb, top], axis=1)


def logsumexp_pair(a, b):
    top = jnp.maximum(a[:, 1:], b[:, 1:])
    mass = a[:, :1] * jnp.exp(a[:, 1:] - top) + b[:, :1] * jnp.exp(b[:, 1:] - top)
    return jnp.concatenate([mass, top], axis=1)


def make_body(size, split):
    bits = list(range(size.bit_length() - 1))
    scatter_bits, double_bits = bits[:split], bits[split:]

    def on_device(table, relations, anchor, rel_one, rel_two):
        rows = table.shape[0]
        idx = lax.axis_index("ent")
        start = idx * rows
        offset = anchor - start
        inside = ((offset >= 0) & (offset < rows)).astype(jnp.float32)
        local_rows = jnp.take(table, jnp.clip(offset, 0, rows - 1), axis=0) * inside[:, None]
        rep = axis_size("rep")
        rep_bits = list(range(rep.bit_length() - 1))
        rel_all = gather_rounds(relations, rep_bits[::-1], lax.axis_index("rep"), "rep")
        rel_first = jnp.take(rel_all, rel_one, axis=0)
        rel_second = jnp.take(rel_all, rel_two, axis=0)

        anchor_block, at = scatter_rounds(local_rows, add_pair, scatter_bits, idx, "ent")
        anchor_block = doubling_rounds(anchor_block, add_pair, double_bits, "ent")
        block = anchor_block.shape[0]
        query_block = cmul(anchor_block, lax.dynamic_slice_in_dim(rel_first, at, block, 0))
        query_one = gather_rounds(query_block, scatter_bits, idx, "ent")

        scores = against(query_one, table)
        peak = jnp.max(scores, axis=1, keepdims=True)
        weights = jnp.exp(scores - peak)
        total = jnp.sum(weights, axis=1, keepdims=True)
        summed = weighted(weights, table)
        state = jnp.concatenate([summed, total, peak], axis=1)
        state, at = scatter_rounds(state, softmax_pair, scatter_bits, idx, "ent")
        state = doubling_rounds(state, softmax_pair, double_bits, "ent")
        expected = state[:, :-2] / state[:, -2:-1]
        query_two = gather_rounds(
            cmul(expected, lax.dynamic_slice_in_dim(rel_second, at, block, 0)), scatter_bits, idx, "ent"
        )

        scores_two = against(query_two, table)
        top = jnp.max(scores_two, axis=1, keepdims=True)
        mass = jnp.sum(jnp.exp(scores_two - top), axis=1, keepdims=True)
        state = doubling_rounds(jnp.concatenate([mass, top], axis=1), logsumexp_pair, bits, "ent")
        return (scores_two - state[:, 1:]) - jnp.log(state[:, :1])

    return on_device


SPLIT = 3


def solution(mesh):
    size = mesh.shape["ent"]
    assert size & (size - 1) == 0 and mesh.shape["rep"] & (mesh.shape["rep"] - 1) == 0
    SIZES.update(mesh.shape)
    in_specs = (P("ent", None), P("rep", None), P("rep"), P("rep"), P("rep"))
    out_specs = P("rep", "ent")
    return jax.shard_map(
        make_body(size, SPLIT), mesh=mesh, in_specs=in_specs, out_specs=out_specs, check_vma=False
    )
```

```python
import jax
import jax.numpy as jnp
from jax import lax
from jax.sharding import PartitionSpec as P


def cmul(left, right):
    half = left.shape[1] // 2
    lre, lim = (left[:, :half], left[:, half:])
    rre, rim = (right[:, :half], right[:, half:])
    return jnp.concatenate([lre * rre - lim * rim, lre * rim + lim * rre], axis=1)


def against(query, table):
    return lax.dot_general(
        query,
        table,
        (((1,), (1,)), ((), ())),
        precision=lax.Precision.HIGHEST,
        preferred_element_type=jnp.float32,
    )


def weighted(weights, table):
    return jnp.dot(
        weights, table, precision=lax.Precision.HIGHEST, preferred_element_type=jnp.float32
    )


def partner(size, group, j):
    mask = sum(((j >> i) & 1) << b for i, b in enumerate(group))
    return [(i, i ^ mask) for i in range(size)]


def digit(idx, group):
    return sum(((idx >> b) & 1) << i for i, b in enumerate(group))


def tree(combine, parts):
    while len(parts) > 1:
        parts = [combine(*parts[i : i + 2]) if i + 1 < len(parts) else parts[i] for i in range(0, len(parts), 2)]
    return parts[0]


def scatter_rounds(state, combine, groups, idx, axis):
    offset = 0
    for group in groups:
        radix = 1 << len(group)
        rows = state.shape[0] // radix
        own = digit(idx, group)
        parts = [lax.dynamic_slice_in_dim(state, own * rows, rows, 0)]
        for j in range(1, radix):
            send = lax.dynamic_slice_in_dim(state, (own ^ j) * rows, rows, 0)
            parts.append(lax.ppermute(send, axis, partner(axis_size(axis), group, j)))
        state = tree(combine, parts)
        offset = offset + own * rows
    return state, offset


def doubling_rounds(state, combine, groups, axis):
    for group in groups:
        parts = [state] + [
            lax.ppermute(state, axis, partner(axis_size(axis), group, j)) for j in range(1, 1 << len(group))
        ]
        state = tree(combine, parts)
    return state


def gather_rounds(block, groups, idx, axis):
    for group in reversed(groups):
        radix = 1 << len(group)
        own = digit(idx, group)
        cases = [block] + [
            lax.ppermute(block, axis, partner(axis_size(axis), group, j)) for j in range(1, radix)
        ]
        block = jnp.concatenate([lax.select_n(p ^ own, *cases) for p in range(radix)], axis=0)
    return block


def bit_groups(size, width):
    bits = list(range(size.bit_length() - 1))
    return [bits[i : i + width] for i in range(0, len(bits), width)]


SIZES = {}


def axis_size(axis):
    return SIZES[axis]


def add_pair(a, b):
    return a + b


def softmax_pair(a, b):
    top = jnp.maximum(a[:, -1:], b[:, -1:])
    fa = jnp.exp(a[:, -1:] - top)
    fb = jnp.exp(b[:, -1:] - top)
    return jnp.concatenate([a[:, :-1] * fa + b[:, :-1] * fb, top], axis=1)


def logsumexp_pair(a, b):
    top = jnp.maximum(a[:, 1:], b[:, 1:])
    mass = a[:, :1] * jnp.exp(a[:, 1:] - top) + b[:, :1] * jnp.exp(b[:, 1:] - top)
    return jnp.concatenate([mass, top], axis=1)


def make_body(size, split):
    groups = bit_groups(size, RADIX_BITS)
    scatter_bits, double_bits = groups[:split], groups[split:]

    def on_device(table, relations, anchor, rel_one, rel_two):
        rows = table.shape[0]
        idx = lax.axis_index("ent")
        start = idx * rows
        offset = anchor - start
        inside = ((offset >= 0) & (offset < rows)).astype(jnp.float32)
        local_rows = jnp.take(table, jnp.clip(offset, 0, rows - 1), axis=0) * inside[:, None]
        rep_groups = bit_groups(axis_size("rep"), RADIX_BITS)
        rel_all = gather_rounds(relations, rep_groups[::-1], lax.axis_index("rep"), "rep")
        rel_first = jnp.take(rel_all, rel_one, axis=0)
        rel_second = jnp.take(rel_all, rel_two, axis=0)

        anchor_block, at = scatter_rounds(local_rows, add_pair, scatter_bits, idx, "ent")
        anchor_block = doubling_rounds(anchor_block, add_pair, double_bits, "ent")
        block = anchor_block.shape[0]
        query_block = cmul(anchor_block, lax.dynamic_slice_in_dim(rel_first, at, block, 0))
        query_one = lax.optimization_barrier(gather_rounds(query_block, scatter_bits, idx, "ent"))

        scores = against(query_one, table)
        peak = jnp.max(scores, axis=1, keepdims=True)
        weights = jnp.exp(scores - peak)
        total = jnp.sum(weights, axis=1, keepdims=True)
        summed = weighted(weights, table)
        state = jnp.concatenate([summed, total, peak], axis=1)
        state, at = scatter_rounds(state, softmax_pair, scatter_bits, idx, "ent")
        state = doubling_rounds(state, softmax_pair, double_bits, "ent")
        expected = state[:, :-2] / state[:, -2:-1]
        query_two = gather_rounds(
            cmul(expected, lax.dynamic_slice_in_dim(rel_second, at, block, 0)), scatter_bits, idx, "ent"
        )
        query_two = lax.optimization_barrier(query_two)

        scores_two = against(query_two, table)
        top = jnp.max(scores_two, axis=1, keepdims=True)
        mass = jnp.sum(jnp.exp(scores_two - top), axis=1, keepdims=True)
        state = doubling_rounds(jnp.concatenate([mass, top], axis=1), logsumexp_pair, groups, "ent")
        return (scores_two - state[:, 1:]) - jnp.log(state[:, :1])

    return on_device


SPLIT = 2
RADIX_BITS = 2


def solution(mesh):
    size = mesh.shape["ent"]
    assert size & (size - 1) == 0 and mesh.shape["rep"] & (mesh.shape["rep"] - 1) == 0
    SIZES.update(mesh.shape)
    in_specs = (P("ent", None), P("rep", None), P("rep"), P("rep"), P("rep"))
    out_specs = P("rep", "ent")
    return jax.shard_map(
        make_body(size, SPLIT), mesh=mesh, in_specs=in_specs, out_specs=out_specs, check_vma=False
    )
```

```python
import jax
import jax.numpy as jnp
from jax import lax
from jax.sharding import PartitionSpec as P


def cmul(left, right):
    half = left.shape[1] // 2
    lre, lim = (left[:, :half], left[:, half:])
    rre, rim = (right[:, :half], right[:, half:])
    return jnp.concatenate([lre * rre - lim * rim, lre * rim + lim * rre], axis=1)


def against(query, table):
    return lax.dot_general(
        query,
        table,
        (((1,), (1,)), ((), ())),
        precision=lax.Precision.HIGHEST,
        preferred_element_type=jnp.float32,
    )


def weighted(weights, table):
    return jnp.dot(
        weights, table, precision=lax.Precision.HIGHEST, preferred_element_type=jnp.float32
    )


def partner(size, group, j):
    mask = sum(((j >> i) & 1) << b for i, b in enumerate(group))
    return [(i, i ^ mask) for i in range(size)]


def digit(idx, group):
    return sum(((idx >> b) & 1) << i for i, b in enumerate(group))


def tree(combine, parts):
    while len(parts) > 1:
        parts = [combine(*parts[i : i + 2]) if i + 1 < len(parts) else parts[i] for i in range(0, len(parts), 2)]
    return parts[0]


def scatter_rounds(state, combine, groups, idx, axis):
    offset = 0
    for group in groups:
        radix = 1 << len(group)
        rows = state.shape[0] // radix
        own = digit(idx, group)
        parts = [lax.dynamic_slice_in_dim(state, own * rows, rows, 0)]
        for j in range(1, radix):
            send = lax.dynamic_slice_in_dim(state, (own ^ j) * rows, rows, 0)
            parts.append(lax.ppermute(send, axis, partner(axis_size(axis), group, j)))
        state = tree(combine, parts)
        offset = offset + own * rows
    return state, offset


def doubling_rounds(state, combine, groups, axis):
    for group in groups:
        parts = [state] + [
            lax.ppermute(state, axis, partner(axis_size(axis), group, j)) for j in range(1, 1 << len(group))
        ]
        state = tree(combine, parts)
    return state


def gather_rounds(block, groups, idx, axis):
    for group in reversed(groups):
        radix = 1 << len(group)
        own = digit(idx, group)
        cases = [block] + [
            lax.ppermute(block, axis, partner(axis_size(axis), group, j)) for j in range(1, radix)
        ]
        block = jnp.concatenate([lax.select_n(p ^ own, *cases) for p in range(radix)], axis=0)
    return block


def bit_groups(size, width):
    bits = list(range(size.bit_length() - 1))
    return [bits[i : i + width] for i in range(0, len(bits), width)]


SIZES = {}


def axis_size(axis):
    return SIZES[axis]


def add_pair(a, b):
    return a + b


def softmax_pair(a, b):
    top = jnp.maximum(a[:, -1:], b[:, -1:])
    fa = jnp.exp(a[:, -1:] - top)
    fb = jnp.exp(b[:, -1:] - top)
    return jnp.concatenate([a[:, :-1] * fa + b[:, :-1] * fb, top], axis=1)


def logsumexp_pair(a, b):
    top = jnp.maximum(a[:, 1:], b[:, 1:])
    mass = a[:, :1] * jnp.exp(a[:, 1:] - top) + b[:, :1] * jnp.exp(b[:, 1:] - top)
    return jnp.concatenate([mass, top], axis=1)


def make_body(size, split):
    groups = bit_groups(size, RADIX_BITS)
    scatter_bits, double_bits = groups[:split], groups[split:]

    def on_device(table, relations, anchor, rel_one, rel_two):
        rows = table.shape[0]
        idx = lax.axis_index("ent")
        start = idx * rows
        offset = anchor - start
        inside = ((offset >= 0) & (offset < rows)).astype(jnp.float32)
        local_rows = jnp.take(table, jnp.clip(offset, 0, rows - 1), axis=0) * inside[:, None]
        rep_groups = bit_groups(axis_size("rep"), RADIX_BITS)
        rel_all = gather_rounds(relations, rep_groups[::-1], lax.axis_index("rep"), "rep")
        rel_first = jnp.take(rel_all, rel_one, axis=0)
        rel_second = jnp.take(rel_all, rel_two, axis=0)

        anchor_block, at = scatter_rounds(local_rows, add_pair, scatter_bits, idx, "ent")
        anchor_block = doubling_rounds(anchor_block, add_pair, double_bits, "ent")
        block = anchor_block.shape[0]
        query_block = cmul(anchor_block, lax.dynamic_slice_in_dim(rel_first, at, block, 0))
        query_one = lax.optimization_barrier(gather_rounds(query_block, scatter_bits, idx, "ent"))

        scores = against(query_one, table)
        peak = jnp.max(scores, axis=1, keepdims=True)
        weights = jnp.exp(scores - peak)
        total = jnp.sum(weights, axis=1, keepdims=True)
        summed = weighted(weights, table)
        state = jnp.concatenate([summed, total, peak], axis=1)
        state, at = scatter_rounds(state, softmax_pair, scatter_bits, idx, "ent")
        state = doubling_rounds(state, softmax_pair, double_bits, "ent")
        expected = state[:, :-2] / state[:, -2:-1]
        query_two = gather_rounds(
            cmul(expected, lax.dynamic_slice_in_dim(rel_second, at, block, 0)), scatter_bits, idx, "ent"
        )
        query_two = lax.optimization_barrier(query_two)

        scores_two = against(query_two, table)
        top = jnp.max(scores_two, axis=1, keepdims=True)
        mass = jnp.sum(jnp.exp(scores_two - top), axis=1, keepdims=True)
        state = doubling_rounds(jnp.concatenate([mass, top], axis=1), logsumexp_pair, groups, "ent")
        return (scores_two - state[:, 1:]) - jnp.log(state[:, :1])

    return on_device


SPLIT = 3
RADIX_BITS = 1


def solution(mesh):
    size = mesh.shape["ent"]
    assert size & (size - 1) == 0 and mesh.shape["rep"] & (mesh.shape["rep"] - 1) == 0
    SIZES.update(mesh.shape)
    in_specs = (P("ent", None), P("rep", None), P("rep"), P("rep"), P("rep"))
    out_specs = P("rep", "ent")
    return jax.shard_map(
        make_body(size, SPLIT), mesh=mesh, in_specs=in_specs, out_specs=out_specs, check_vma=False
    )
```

```python
import jax
import jax.numpy as jnp
from jax import lax
from jax.sharding import PartitionSpec as P


def cmul(left, right):
    half = left.shape[1] // 2
    lre, lim = (left[:, :half], left[:, half:])
    rre, rim = (right[:, :half], right[:, half:])
    return jnp.concatenate([lre * rre - lim * rim, lre * rim + lim * rre], axis=1)


def against(query, table):
    return lax.dot_general(
        query,
        table,
        (((1,), (1,)), ((), ())),
        precision=lax.Precision.HIGHEST,
        preferred_element_type=jnp.float32,
    )


def weighted(weights, table):
    return jnp.dot(
        weights, table, precision=lax.Precision.HIGHEST, preferred_element_type=jnp.float32
    )


def partner(size, group, j):
    mask = sum(((j >> i) & 1) << b for i, b in enumerate(group))
    return [(i, i ^ mask) for i in range(size)]


def digit(idx, group):
    return sum(((idx >> b) & 1) << i for i, b in enumerate(group))


def tree(combine, parts):
    while len(parts) > 1:
        parts = [combine(*parts[i : i + 2]) if i + 1 < len(parts) else parts[i] for i in range(0, len(parts), 2)]
    return parts[0]


def scatter_rounds(state, combine, groups, idx, axis):
    offset = 0
    for group in groups:
        radix = 1 << len(group)
        rows = state.shape[0] // radix
        own = digit(idx, group)
        parts = [lax.dynamic_slice_in_dim(state, own * rows, rows, 0)]
        for j in range(1, radix):
            send = lax.dynamic_slice_in_dim(state, (own ^ j) * rows, rows, 0)
            parts.append(lax.ppermute(send, axis, partner(axis_size(axis), group, j)))
        state = tree(combine, parts)
        offset = offset + own * rows
    return state, offset


def doubling_rounds(state, combine, groups, axis):
    for group in groups:
        parts = [state] + [
            lax.ppermute(state, axis, partner(axis_size(axis), group, j)) for j in range(1, 1 << len(group))
        ]
        state = tree(combine, parts)
    return state


def gather_rounds(block, groups, idx, axis):
    for group in reversed(groups):
        radix = 1 << len(group)
        own = digit(idx, group)
        cases = [block] + [
            lax.ppermute(block, axis, partner(axis_size(axis), group, j)) for j in range(1, radix)
        ]
        block = jnp.concatenate([lax.select_n(p ^ own, *cases) for p in range(radix)], axis=0)
    return block


def bit_groups(size, width):
    bits = list(range(size.bit_length() - 1))
    return [bits[i : i + width] for i in range(0, len(bits), width)]


SIZES = {}


def axis_size(axis):
    return SIZES[axis]


def add_pair(a, b):
    return a + b


def softmax_pair(a, b):
    top = jnp.maximum(a[:, -1:], b[:, -1:])
    fa = jnp.exp(a[:, -1:] - top)
    fb = jnp.exp(b[:, -1:] - top)
    return jnp.concatenate([a[:, :-1] * fa + b[:, :-1] * fb, top], axis=1)


def logsumexp_pair(a, b):
    top = jnp.maximum(a[:, 1:], b[:, 1:])
    mass = a[:, :1] * jnp.exp(a[:, 1:] - top) + b[:, :1] * jnp.exp(b[:, 1:] - top)
    return jnp.concatenate([mass, top], axis=1)


def first_hop(query, table):
    scores = against(query, table)
    peak = jnp.max(scores, axis=1, keepdims=True)
    weights = jnp.exp(scores - peak)
    total = jnp.sum(weights, axis=1, keepdims=True)
    return jnp.concatenate([weighted(weights, table), total, peak], axis=1)


def second_hop(query, table):
    scores = against(query, table)
    top = jnp.max(scores, axis=1, keepdims=True)
    mass = jnp.sum(jnp.exp(scores - top), axis=1, keepdims=True)
    return scores, jnp.concatenate([mass, top], axis=1)


def make_body(size, split):
    groups = bit_groups(size, RADIX_BITS)
    scatter_bits, double_bits = groups[:split], groups[split:]
    hop_groups = scatter_bits[1:2] + scatter_bits[:1] + scatter_bits[2:]

    def on_device(table, relations, anchor, rel_one, rel_two):
        rows = table.shape[0]
        idx = lax.axis_index("ent")
        start = idx * rows
        offset = anchor - start
        inside = ((offset >= 0) & (offset < rows)).astype(jnp.float32)
        local_rows = jnp.take(table, jnp.clip(offset, 0, rows - 1), axis=0) * inside[:, None]
        rep_groups = bit_groups(axis_size("rep"), RADIX_BITS)
        rel_all = gather_rounds(relations, rep_groups[::-1], lax.axis_index("rep"), "rep")
        rel_first = jnp.take(rel_all, rel_one, axis=0)
        rel_second = jnp.take(rel_all, rel_two, axis=0)

        anchor_block, at = scatter_rounds(local_rows, add_pair, scatter_bits, idx, "ent")
        anchor_block = doubling_rounds(anchor_block, add_pair, double_bits, "ent")
        block = anchor_block.shape[0]
        query_block = cmul(anchor_block, lax.dynamic_slice_in_dim(rel_first, at, block, 0))
        query_one = gather_rounds(query_block, scatter_bits, idx, "ent")

        first = hop_groups[0]
        side = digit(idx, first)
        half = query_one.shape[0] // 2
        sent = lax.ppermute(
            first_hop(lax.dynamic_slice_in_dim(query_one, (1 - side) * half, half, 0), table),
            "ent",
            partner(size, first, 1),
        )
        state = softmax_pair(first_hop(lax.dynamic_slice_in_dim(query_one, side * half, half, 0), table), sent)
        state, at = scatter_rounds(state, softmax_pair, hop_groups[1:], idx, "ent")
        at = at + side * half
        state = doubling_rounds(state, softmax_pair, double_bits, "ent")
        expected = state[:, :-2] / state[:, -2:-1]
        block_two = cmul(expected, lax.dynamic_slice_in_dim(rel_second, at, block, 0))
        own = gather_rounds(block_two, hop_groups[1:], idx, "ent")

        other = lax.ppermute(own, "ent", partner(size, first, 1))
        own_scores, own_stat = second_hop(own, table)
        other_scores, other_stat = second_hop(other, table)
        low = jnp.where(side == 0, own_stat, other_stat)
        high = jnp.where(side == 0, other_stat, own_stat)
        stat = doubling_rounds(jnp.concatenate([low, high], axis=0), logsumexp_pair, groups, "ent")
        own_stat = lax.dynamic_slice_in_dim(stat, side * half, half, 0)
        other_stat = lax.dynamic_slice_in_dim(stat, (1 - side) * half, half, 0)
        own_out = (own_scores - own_stat[:, 1:]) - jnp.log(own_stat[:, :1])
        other_out = (other_scores - other_stat[:, 1:]) - jnp.log(other_stat[:, :1])
        both = jnp.concatenate([own_out, other_out, own_out], axis=0)
        return lax.dynamic_slice_in_dim(both, side * half, 2 * half, 0)

    return on_device


SPLIT = 3
RADIX_BITS = 1


def solution(mesh):
    size = mesh.shape["ent"]
    assert size & (size - 1) == 0 and mesh.shape["rep"] & (mesh.shape["rep"] - 1) == 0
    SIZES.update(mesh.shape)
    in_specs = (P("ent", None), P("rep", None), P("rep"), P("rep"), P("rep"))
    out_specs = P("rep", "ent")
    return jax.shard_map(
        make_body(size, SPLIT), mesh=mesh, in_specs=in_specs, out_specs=out_specs, check_vma=False
    )
```

```python
import jax
import jax.numpy as jnp
from jax import lax
from jax.experimental.layout import Layout, with_layout_constraint
from jax.sharding import PartitionSpec as P


def cmul(left, right):
    half = left.shape[1] // 2
    lre, lim = (left[:, :half], left[:, half:])
    rre, rim = (right[:, :half], right[:, half:])
    return jnp.concatenate([lre * rre - lim * rim, lre * rim + lim * rre], axis=1)


def against(query, table):
    return lax.dot_general(
        query,
        table,
        (((1,), (1,)), ((), ())),
        precision=lax.Precision.HIGHEST,
        preferred_element_type=jnp.float32,
    )


def weighted(weights, table):
    return jnp.dot(
        weights, table, precision=lax.Precision.HIGHEST, preferred_element_type=jnp.float32
    )


def row_major(x):
    return with_layout_constraint(x, Layout(major_to_minor=tuple(range(x.ndim))))


def partner(size, group, j):
    mask = sum(((j >> i) & 1) << b for i, b in enumerate(group))
    return [(i, i ^ mask) for i in range(size)]


def digit(idx, group):
    return sum(((idx >> b) & 1) << i for i, b in enumerate(group))


def tree(combine, parts):
    while len(parts) > 1:
        parts = [combine(*parts[i : i + 2]) if i + 1 < len(parts) else parts[i] for i in range(0, len(parts), 2)]
    return parts[0]


def scatter_rounds(state, combine, groups, idx, axis):
    offset = 0
    for group in groups:
        radix = 1 << len(group)
        rows = state.shape[0] // radix
        own = digit(idx, group)
        parts = [lax.dynamic_slice_in_dim(state, own * rows, rows, 0)]
        for j in range(1, radix):
            send = lax.dynamic_slice_in_dim(state, (own ^ j) * rows, rows, 0)
            parts.append(lax.ppermute(send, axis, partner(axis_size(axis), group, j)))
        state = tree(combine, parts)
        offset = offset + own * rows
    return state, offset


def doubling_rounds(state, combine, groups, axis):
    for group in groups:
        parts = [state] + [
            lax.ppermute(state, axis, partner(axis_size(axis), group, j)) for j in range(1, 1 << len(group))
        ]
        state = tree(combine, parts)
    return state


def gather_rounds(block, groups, idx, axis):
    for group in reversed(groups):
        radix = 1 << len(group)
        own = digit(idx, group)
        cases = [block] + [
            lax.ppermute(block, axis, partner(axis_size(axis), group, j)) for j in range(1, radix)
        ]
        block = jnp.concatenate([lax.select_n(p ^ own, *cases) for p in range(radix)], axis=0)
    return block


def bit_groups(size, width):
    bits = list(range(size.bit_length() - 1))
    return [bits[i : i + width] for i in range(0, len(bits), width)]


SIZES = {}


def axis_size(axis):
    return SIZES[axis]


def add_pair(a, b):
    return a + b


def softmax_pair(a, b):
    top = jnp.maximum(a[:, -1:], b[:, -1:])
    fa = jnp.exp(a[:, -1:] - top)
    fb = jnp.exp(b[:, -1:] - top)
    return jnp.concatenate([a[:, :-1] * fa + b[:, :-1] * fb, top], axis=1)


def logsumexp_pair(a, b):
    top = jnp.maximum(a[:, 1:], b[:, 1:])
    mass = a[:, :1] * jnp.exp(a[:, 1:] - top) + b[:, :1] * jnp.exp(b[:, 1:] - top)
    return jnp.concatenate([mass, top], axis=1)


def make_body(size, split):
    groups = bit_groups(size, RADIX_BITS)
    scatter_bits, double_bits = groups[:split], groups[split:]

    def on_device(table, relations, anchor, rel_one, rel_two):
        rows = table.shape[0]
        idx = lax.axis_index("ent")
        start = idx * rows
        offset = anchor - start
        inside = ((offset >= 0) & (offset < rows)).astype(jnp.float32)
        local_rows = jnp.take(table, jnp.clip(offset, 0, rows - 1), axis=0) * inside[:, None]
        rep_groups = bit_groups(axis_size("rep"), RADIX_BITS)
        rel_all = gather_rounds(relations, rep_groups[::-1], lax.axis_index("rep"), "rep")
        rel_first = jnp.take(rel_all, rel_one, axis=0)
        rel_second = jnp.take(rel_all, rel_two, axis=0)

        anchor_block, at = scatter_rounds(local_rows, add_pair, scatter_bits, idx, "ent")
        anchor_block = doubling_rounds(anchor_block, add_pair, double_bits, "ent")
        block = anchor_block.shape[0]
        query_block = cmul(anchor_block, lax.dynamic_slice_in_dim(rel_first, at, block, 0))
        query_one = row_major(gather_rounds(query_block, scatter_bits, idx, "ent"))

        scores = against(query_one, table)
        peak = jnp.max(scores, axis=1, keepdims=True)
        weights = jnp.exp(scores - peak)
        total = jnp.sum(weights, axis=1, keepdims=True)
        summed = weighted(weights, table)
        state = jnp.concatenate([summed, total, peak], axis=1)
        state, at = scatter_rounds(state, softmax_pair, scatter_bits, idx, "ent")
        state = doubling_rounds(state, softmax_pair, double_bits, "ent")
        expected = state[:, :-2] / state[:, -2:-1]
        query_two = gather_rounds(
            cmul(expected, lax.dynamic_slice_in_dim(rel_second, at, block, 0)), scatter_bits, idx, "ent"
        )
        query_two = row_major(query_two)

        scores_two = against(query_two, table)
        top = jnp.max(scores_two, axis=1, keepdims=True)
        mass = jnp.sum(jnp.exp(scores_two - top), axis=1, keepdims=True)
        state = doubling_rounds(jnp.concatenate([mass, top], axis=1), logsumexp_pair, groups, "ent")
        return (scores_two - state[:, 1:]) - jnp.log(state[:, :1])

    return on_device


SPLIT = 3
RADIX_BITS = 1


def solution(mesh):
    size = mesh.shape["ent"]
    assert size & (size - 1) == 0 and mesh.shape["rep"] & (mesh.shape["rep"] - 1) == 0
    SIZES.update(mesh.shape)
    in_specs = (P("ent", None), P("rep", None), P("rep"), P("rep"), P("rep"))
    out_specs = P("rep", "ent")
    return jax.shard_map(
        make_body(size, SPLIT), mesh=mesh, in_specs=in_specs, out_specs=out_specs, check_vma=False
    )
```

```python
import jax
import jax.numpy as jnp
from jax import lax
from jax.experimental.layout import Layout, with_layout_constraint
from jax.sharding import PartitionSpec as P


def cmul(left, right):
    half = left.shape[1] // 2
    lre, lim = (left[:, :half], left[:, half:])
    rre, rim = (right[:, :half], right[:, half:])
    return jnp.concatenate([lre * rre - lim * rim, lre * rim + lim * rre], axis=1)


def against(query, table):
    return lax.dot_general(
        query,
        table,
        (((1,), (1,)), ((), ())),
        precision=lax.Precision.HIGHEST,
        preferred_element_type=jnp.float32,
    )


def weighted(weights, table):
    return jnp.dot(
        weights, table, precision=lax.Precision.HIGHEST, preferred_element_type=jnp.float32
    )


def row_major(x):
    return with_layout_constraint(x, Layout(major_to_minor=tuple(range(x.ndim))))


def partner(size, group, j):
    mask = sum(((j >> i) & 1) << b for i, b in enumerate(group))
    return [(i, i ^ mask) for i in range(size)]


def digit(idx, group):
    return sum(((idx >> b) & 1) << i for i, b in enumerate(group))


def tree(combine, parts):
    while len(parts) > 1:
        parts = [combine(*parts[i : i + 2]) if i + 1 < len(parts) else parts[i] for i in range(0, len(parts), 2)]
    return parts[0]


def scatter_rounds(state, combine, groups, idx, axis):
    offset = 0
    for group in groups:
        radix = 1 << len(group)
        rows = state.shape[0] // radix
        own = digit(idx, group)
        parts = [lax.dynamic_slice_in_dim(state, own * rows, rows, 0)]
        for j in range(1, radix):
            send = lax.dynamic_slice_in_dim(state, (own ^ j) * rows, rows, 0)
            parts.append(lax.ppermute(send, axis, partner(axis_size(axis), group, j)))
        state = tree(combine, parts)
        offset = offset + own * rows
    return state, offset


def doubling_rounds(state, combine, groups, axis):
    for group in groups:
        parts = [state] + [
            lax.ppermute(state, axis, partner(axis_size(axis), group, j)) for j in range(1, 1 << len(group))
        ]
        state = tree(combine, parts)
    return state


def gather_rounds(block, groups, idx, axis):
    for group in reversed(groups):
        radix = 1 << len(group)
        own = digit(idx, group)
        cases = [block] + [
            lax.ppermute(block, axis, partner(axis_size(axis), group, j)) for j in range(1, radix)
        ]
        block = jnp.concatenate([lax.select_n(p ^ own, *cases) for p in range(radix)], axis=0)
    return block


def bit_groups(size, width):
    bits = list(range(size.bit_length() - 1))
    return [bits[i : i + width] for i in range(0, len(bits), width)]


SIZES = {}


def axis_size(axis):
    return SIZES[axis]


def add_pair(a, b):
    return a + b


def softmax_pair(a, b):
    top = jnp.maximum(a[:, -1:], b[:, -1:])
    fa = jnp.exp(a[:, -1:] - top)
    fb = jnp.exp(b[:, -1:] - top)
    return jnp.concatenate([a[:, :-1] * fa + b[:, :-1] * fb, top], axis=1)


def logsumexp_pair(a, b):
    top = jnp.maximum(a[:, 1:], b[:, 1:])
    mass = a[:, :1] * jnp.exp(a[:, 1:] - top) + b[:, :1] * jnp.exp(b[:, 1:] - top)
    return jnp.concatenate([mass, top], axis=1)


def make_body(size, split):
    groups = bit_groups(size, RADIX_BITS)
    scatter_bits, double_bits = groups[:split], groups[split:]

    def on_device(table, relations, anchor, rel_one, rel_two):
        rows = table.shape[0]
        idx = lax.axis_index("ent")
        start = idx * rows
        offset = anchor - start
        inside = ((offset >= 0) & (offset < rows)).astype(jnp.float32)
        local_rows = jnp.take(table, jnp.clip(offset, 0, rows - 1), axis=0) * inside[:, None]
        rep_groups = bit_groups(axis_size("rep"), RADIX_BITS)
        rel_all = gather_rounds(relations, rep_groups[::-1], lax.axis_index("rep"), "rep")
        rel_first = jnp.take(rel_all, rel_one, axis=0)
        rel_second = jnp.take(rel_all, rel_two, axis=0)

        anchor_block, at = scatter_rounds(local_rows, add_pair, scatter_bits, idx, "ent")
        anchor_block = doubling_rounds(anchor_block, add_pair, double_bits, "ent")
        block = anchor_block.shape[0]
        query_one = row_major(cmul(gather_rounds(anchor_block, scatter_bits, idx, "ent"), rel_first))

        scores = against(query_one, table)
        peak = jnp.max(scores, axis=1, keepdims=True)
        weights = jnp.exp(scores - peak)
        total = jnp.sum(weights, axis=1, keepdims=True)
        summed = weighted(weights, table)
        state = jnp.concatenate([summed, total, peak], axis=1)
        state, at = scatter_rounds(state, softmax_pair, scatter_bits, idx, "ent")
        state = doubling_rounds(state, softmax_pair, double_bits, "ent")
        expected = state[:, :-2] / state[:, -2:-1]
        query_two = gather_rounds(
            cmul(expected, lax.dynamic_slice_in_dim(rel_second, at, block, 0)), scatter_bits, idx, "ent"
        )
        query_two = row_major(query_two)

        scores_two = against(query_two, table)
        top = jnp.max(scores_two, axis=1, keepdims=True)
        mass = jnp.sum(jnp.exp(scores_two - top), axis=1, keepdims=True)
        state = doubling_rounds(jnp.concatenate([mass, top], axis=1), logsumexp_pair, groups, "ent")
        return (scores_two - state[:, 1:]) - jnp.log(state[:, :1])

    return on_device


SPLIT = 3
RADIX_BITS = 1


def solution(mesh):
    size = mesh.shape["ent"]
    assert size & (size - 1) == 0 and mesh.shape["rep"] & (mesh.shape["rep"] - 1) == 0
    SIZES.update(mesh.shape)
    in_specs = (P("ent", None), P("rep", None), P("rep"), P("rep"), P("rep"))
    out_specs = P("rep", "ent")
    return jax.shard_map(
        make_body(size, SPLIT), mesh=mesh, in_specs=in_specs, out_specs=out_specs, check_vma=False
    )
```

```python
import jax
import jax.numpy as jnp
from jax import lax
from jax.experimental.layout import Layout, with_layout_constraint
from jax.sharding import PartitionSpec as P


def cmul(left, right):
    half = left.shape[1] // 2
    lre, lim = (left[:, :half], left[:, half:])
    rre, rim = (right[:, :half], right[:, half:])
    return jnp.concatenate([lre * rre - lim * rim, lre * rim + lim * rre], axis=1)


def against(query, table):
    return lax.dot_general(
        query,
        table,
        (((1,), (1,)), ((), ())),
        precision=lax.Precision.HIGHEST,
        preferred_element_type=jnp.float32,
    )


def weighted(weights, table):
    return jnp.dot(
        weights, table, precision=lax.Precision.HIGHEST, preferred_element_type=jnp.float32
    )


def row_major(x):
    return with_layout_constraint(x, Layout(major_to_minor=tuple(range(x.ndim))))


def partner(size, group, j):
    mask = sum(((j >> i) & 1) << b for i, b in enumerate(group))
    return [(i, i ^ mask) for i in range(size)]


def digit(idx, group):
    return sum(((idx >> b) & 1) << i for i, b in enumerate(group))


def tree(combine, parts):
    while len(parts) > 1:
        parts = [combine(*parts[i : i + 2]) if i + 1 < len(parts) else parts[i] for i in range(0, len(parts), 2)]
    return parts[0]


def scatter_rounds(state, combine, groups, idx, axis):
    offset = 0
    for group in groups:
        radix = 1 << len(group)
        rows = state.shape[0] // radix
        own = digit(idx, group)
        parts = [lax.dynamic_slice_in_dim(state, own * rows, rows, 0)]
        for j in range(1, radix):
            send = lax.dynamic_slice_in_dim(state, (own ^ j) * rows, rows, 0)
            parts.append(lax.ppermute(send, axis, partner(axis_size(axis), group, j)))
        state = tree(combine, parts)
        offset = offset + own * rows
    return state, offset


def doubling_rounds(state, combine, groups, axis):
    for group in groups:
        parts = [state] + [
            lax.ppermute(state, axis, partner(axis_size(axis), group, j)) for j in range(1, 1 << len(group))
        ]
        state = tree(combine, parts)
    return state


def gather_rounds(block, groups, idx, axis):
    for group in reversed(groups):
        radix = 1 << len(group)
        own = digit(idx, group)
        cases = [block] + [
            lax.ppermute(block, axis, partner(axis_size(axis), group, j)) for j in range(1, radix)
        ]
        block = jnp.concatenate([lax.select_n(p ^ own, *cases) for p in range(radix)], axis=0)
    return block


def bit_groups(size, width):
    bits = list(range(size.bit_length() - 1))
    return [bits[i : i + width] for i in range(0, len(bits), width)]


SIZES = {}


def axis_size(axis):
    return SIZES[axis]


def add_pair(a, b):
    return a + b


def softmax_pair(a, b):
    top = jnp.maximum(a[:, -1:], b[:, -1:])
    fa = jnp.exp(a[:, -1:] - top)
    fb = jnp.exp(b[:, -1:] - top)
    return jnp.concatenate([a[:, :-1] * fa + b[:, :-1] * fb, top], axis=1)


def logsumexp_pair(a, b):
    top = jnp.maximum(a[:, 1:], b[:, 1:])
    mass = a[:, :1] * jnp.exp(a[:, 1:] - top) + b[:, :1] * jnp.exp(b[:, 1:] - top)
    return jnp.concatenate([mass, top], axis=1)


def make_body(size, split):
    groups = bit_groups(size, RADIX_BITS)
    scatter_bits, double_bits = groups[:split], groups[split:]

    def on_device(table, relations, anchor, rel_one, rel_two):
        rows = table.shape[0]
        idx = lax.axis_index("ent")
        start = idx * rows
        offset = anchor - start
        inside = ((offset >= 0) & (offset < rows)).astype(jnp.float32)
        local_rows = jnp.take(table, jnp.clip(offset, 0, rows - 1), axis=0) * inside[:, None]
        rep_groups = bit_groups(axis_size("rep"), RADIX_BITS)
        rel_all = gather_rounds(relations, rep_groups[::-1], lax.axis_index("rep"), "rep")
        rel_first = jnp.take(rel_all, rel_one, axis=0)
        rel_second = jnp.take(rel_all, rel_two, axis=0)

        anchor_block, at = scatter_rounds(local_rows, add_pair, scatter_bits, idx, "ent")
        anchor_block = doubling_rounds(anchor_block, add_pair, double_bits, "ent")
        block = anchor_block.shape[0]
        query_one = row_major(cmul(gather_rounds(anchor_block, scatter_bits, idx, "ent"), rel_first))

        scores = against(query_one, table)
        peak = jnp.max(scores, axis=1, keepdims=True)
        weights = jnp.exp(scores - peak)
        total = jnp.sum(weights, axis=1, keepdims=True)
        summed = weighted(weights, table)
        state = jnp.concatenate([summed, total, peak], axis=1)
        state, at = scatter_rounds(state, softmax_pair, scatter_bits, idx, "ent")
        state = doubling_rounds(state, softmax_pair, double_bits, "ent")
        expected = state[:, :-2] / state[:, -2:-1]
        query_two = gather_rounds(
            cmul(expected, lax.dynamic_slice_in_dim(rel_second, at, block, 0)), scatter_bits, idx, "ent"
        )
        query_two = row_major(query_two)

        scores_two = against(query_two, table)
        top = jnp.max(scores_two, axis=1, keepdims=True)
        mass = jnp.sum(jnp.exp(scores_two - top), axis=1, keepdims=True)
        state = doubling_rounds(jnp.concatenate([mass, top], axis=1), logsumexp_pair, groups, "ent")
        return (scores_two - state[:, 1:]) - jnp.log(state[:, :1])

    return on_device


SPLIT = 2
RADIX_BITS = 1


def solution(mesh):
    size = mesh.shape["ent"]
    assert size & (size - 1) == 0 and mesh.shape["rep"] & (mesh.shape["rep"] - 1) == 0
    SIZES.update(mesh.shape)
    in_specs = (P("ent", None), P("rep", None), P("rep"), P("rep"), P("rep"))
    out_specs = P("rep", "ent")
    return jax.shard_map(
        make_body(size, SPLIT), mesh=mesh, in_specs=in_specs, out_specs=out_specs, check_vma=False
    )
```

```python
import jax
import jax.numpy as jnp
from jax import lax
from jax.experimental.layout import Layout, with_layout_constraint
from jax.sharding import PartitionSpec as P


def cmul(left, right):
    half = left.shape[1] // 2
    lre, lim = (left[:, :half], left[:, half:])
    rre, rim = (right[:, :half], right[:, half:])
    return jnp.concatenate([lre * rre - lim * rim, lre * rim + lim * rre], axis=1)


def against(query, table):
    return lax.dot_general(
        query,
        table,
        (((1,), (1,)), ((), ())),
        precision=lax.Precision.HIGHEST,
        preferred_element_type=jnp.float32,
    )


def weighted(weights, table):
    return jnp.dot(
        weights, table, precision=lax.Precision.HIGHEST, preferred_element_type=jnp.float32
    )


def row_major(x):
    return with_layout_constraint(x, Layout(major_to_minor=tuple(range(x.ndim))))


def partner(size, group, j):
    mask = sum(((j >> i) & 1) << b for i, b in enumerate(group))
    return [(i, i ^ mask) for i in range(size)]


def digit(idx, group):
    return sum(((idx >> b) & 1) << i for i, b in enumerate(group))


def tree(combine, parts):
    while len(parts) > 1:
        parts = [combine(*parts[i : i + 2]) if i + 1 < len(parts) else parts[i] for i in range(0, len(parts), 2)]
    return parts[0]


def scatter_rounds(state, combine, groups, idx, axis):
    offset = 0
    for group in groups:
        radix = 1 << len(group)
        rows = state.shape[0] // radix
        own = digit(idx, group)
        parts = [lax.dynamic_slice_in_dim(state, own * rows, rows, 0)]
        for j in range(1, radix):
            send = lax.dynamic_slice_in_dim(state, (own ^ j) * rows, rows, 0)
            parts.append(lax.ppermute(send, axis, partner(axis_size(axis), group, j)))
        state = tree(combine, parts)
        offset = offset + own * rows
    return state, offset


def doubling_rounds(state, combine, groups, axis):
    for group in groups:
        parts = [state] + [
            lax.ppermute(state, axis, partner(axis_size(axis), group, j)) for j in range(1, 1 << len(group))
        ]
        state = tree(combine, parts)
    return state


def gather_rounds(block, groups, idx, axis):
    for group in reversed(groups):
        radix = 1 << len(group)
        own = digit(idx, group)
        cases = [block] + [
            lax.ppermute(block, axis, partner(axis_size(axis), group, j)) for j in range(1, radix)
        ]
        block = jnp.concatenate([lax.select_n(p ^ own, *cases) for p in range(radix)], axis=0)
    return block


def bit_groups(size, width):
    bits = list(range(size.bit_length() - 1))
    return [bits[i : i + width] for i in range(0, len(bits), width)]


SIZES = {}


def axis_size(axis):
    return SIZES[axis]


def add_pair(a, b):
    return a + b


def softmax_pair(a, b):
    top = jnp.maximum(a[:, -1:], b[:, -1:])
    fa = jnp.exp(a[:, -1:] - top)
    fb = jnp.exp(b[:, -1:] - top)
    return jnp.concatenate([a[:, :-1] * fa + b[:, :-1] * fb, top], axis=1)


def logsumexp_pair(a, b):
    top = jnp.maximum(a[:, 1:], b[:, 1:])
    mass = a[:, :1] * jnp.exp(a[:, 1:] - top) + b[:, :1] * jnp.exp(b[:, 1:] - top)
    return jnp.concatenate([mass, top], axis=1)


def make_body(size, split):
    groups = bit_groups(size, RADIX_BITS)
    scatter_bits, double_bits = groups[:split], groups[split:]

    def on_device(table, relations, anchor, rel_one, rel_two):
        rows = table.shape[0]
        idx = lax.axis_index("ent")
        start = idx * rows
        offset = anchor - start
        inside = ((offset >= 0) & (offset < rows)).astype(jnp.float32)
        local_rows = jnp.take(table, jnp.clip(offset, 0, rows - 1), axis=0) * inside[:, None]
        rep_groups = bit_groups(axis_size("rep"), RADIX_BITS)
        rel_all = gather_rounds(relations, rep_groups[::-1], lax.axis_index("rep"), "rep")
        rel_first = jnp.take(rel_all, rel_one, axis=0)
        rel_second = jnp.take(rel_all, rel_two, axis=0)

        anchor_block, at = scatter_rounds(local_rows, add_pair, scatter_bits, idx, "ent")
        anchor_block = doubling_rounds(anchor_block, add_pair, double_bits, "ent")
        block = anchor_block.shape[0]
        query_block = cmul(anchor_block, lax.dynamic_slice_in_dim(rel_first, at, block, 0))
        query_one = row_major(gather_rounds(query_block, scatter_bits, idx, "ent"))

        scores = against(query_one, table)
        peak = jnp.max(scores, axis=1, keepdims=True)
        weights = jnp.exp(scores - peak)
        total = jnp.sum(weights, axis=1, keepdims=True)
        summed = weighted(weights, table)
        state = jnp.concatenate([summed, total, peak], axis=1)
        state, at = scatter_rounds(state, softmax_pair, scatter_bits, idx, "ent")
        state = doubling_rounds(state, softmax_pair, double_bits, "ent")
        expected = state[:, :-2] / state[:, -2:-1]
        query_two = gather_rounds(
            cmul(expected, lax.dynamic_slice_in_dim(rel_second, at, block, 0)), scatter_bits, idx, "ent"
        )
        query_two = row_major(query_two)

        scores_two = against(query_two, table)
        top = jnp.max(scores_two, axis=1, keepdims=True)
        mass = jnp.sum(jnp.exp(scores_two - top), axis=1, keepdims=True)
        state = doubling_rounds(jnp.concatenate([mass, top], axis=1), logsumexp_pair, groups, "ent")
        return (scores_two - state[:, 1:]) - jnp.log(state[:, :1])

    return on_device


SPLIT = 4
RADIX_BITS = 1


def solution(mesh):
    size = mesh.shape["ent"]
    assert size & (size - 1) == 0 and mesh.shape["rep"] & (mesh.shape["rep"] - 1) == 0
    SIZES.update(mesh.shape)
    in_specs = (P("ent", None), P("rep", None), P("rep"), P("rep"), P("rep"))
    out_specs = P("rep", "ent")
    return jax.shard_map(
        make_body(size, SPLIT), mesh=mesh, in_specs=in_specs, out_specs=out_specs, check_vma=False
    )
```
